512 devices in a mesh: req: 64 (over z, x), head: 8 (over y, core).
Axes of the slice: x: 4, y: 4, z: 16, core: 2. Of those that a mesh axis runs over, the one named last changes fastest.
Arguments:
- tokens: bfloat16 [128, 1024], P('req'), may hold values from -6 to 6
- self_keys: bfloat16 [128, 512, 1024], P('req', None, 'head'), may hold values from -240 to 240
- self_values: bfloat16 [128, 512, 1024], P('req', None, 'head'), may hold values from -6 to 6
- self_len: int32 [128], P('req'), may hold values from 1 to 512, as said below
- cross_keys: bfloat16 [128, 512, 1024], P('req', None, 'head'), may hold values from -240 to 240
- cross_values: bfloat16 [128, 512, 1024], P('req', None, 'head'), may hold values from -6 to 6
- cross_len: int32 [128], P('req'), may hold values from 1 to 512, as said below
- give_slot: int32 [64], P('req'), may hold values from 0 to 1
- w_query: bfloat16 [1024, 1024], P(None, 'head'), may hold values from -0.1875 to 0.1875
- w_key: bfloat16 [1024, 1024], P(None, 'head'), may hold values from -0.1875 to 0.1875
- w_value: bfloat16 [1024, 1024], P(None, 'head'), may hold values from -0.1875 to 0.1875
- w_out: bfloat16 [1024, 1024], P('head'), may hold values from -0.1875 to 0.1875
- w_cross_query: bfloat16 [1024, 1024], P(None, 'head'), may hold values from -0.1875 to 0.1875
- w_cross_out: bfloat16 [1024, 1024], P('head'), may hold values from -0.1875 to 0.1875
- w_up: bfloat16 [1024, 4096], P(None, 'head'), may hold values from -0.1875 to 0.1875
- w_down: bfloat16 [4096, 1024], P('head'), may hold values from -0.09375 to 0.09375
- gain_self: float32 [1024], replicated, may hold values from 0.1 to 1.9
- gain_cross: float32 [1024], replicated, may hold values from 0.1 to 1.9
- gain_final: float32 [1024], replicated, may hold values from 0.1 to 1.9
Outputs:
- decoded: bfloat16 [128, 1024], P('req')
- new_keys: bfloat16 [128, 1024], P('req', 'head')
- new_values: bfloat16 [128, 1024], P('req', 'head')
- moved_keys: bfloat16 [64, 512, 1024], P('req', None, 'head')
- moved_values: bfloat16 [64, 512, 1024], P('req', None, 'head')
The draws below stay inside these ranges and needn't reach their ends.
Inputs may be any that keep to these rules, and one draw needn't show every extreme that they name: `self_len`: each request fills at least one slot; some request fills all 512. `cross_len`: each request has at least one encoder position; some request has 512.
All inputs are finite; a program needn't handle non-finite values.
Results may differ from the reference program's by a relative error of at most 0.039.
Values may be sent and summed in bfloat16 or wider, within the bound.
No kernel may reach another device: no remote copies, remote signals or barrier semaphores. Data moves between devices by JAX's collectives and lax.ppermute only.
A program may use at most 64 MiB of HBM per device.

```python
import jax
import jax.numpy as jnp
from jax import lax

D = 1024
HEADS = 16
HEAD_DIM = 64
FF = 4096
REQ_DEV = 2
S_MAX = 512
E_MAX = 512
REQUESTS = 128
MOVES = 64


def length_draw(key, count, most):
    first_key, second_key, third_key = jax.random.split(key, 3)
    one = jax.random.randint(first_key, (count,), 1, most + 1)
    two = jax.random.randint(second_key, (count,), 1, most + 1)
    lengths = jnp.minimum(one, two)
    spot = jax.random.randint(third_key, (), 0, count)
    return jnp.where(jnp.arange(count) == spot, most, lengths).astype(jnp.int32)


def key_draw(key, count, span):
    base_key = jax.random.fold_in(key, 0)
    values = jax.random.normal(base_key, (count, span, HEADS, HEAD_DIM), jnp.float32)
    values = jnp.clip(values, -4.0, 4.0)
    return values.reshape(count, span, HEADS * HEAD_DIM)


def draw_self_len(key, part):
    return length_draw(jax.random.fold_in(key, 11), REQUESTS, S_MAX)


def draw_cross_len(key, part):
    return length_draw(jax.random.fold_in(key, 13), REQUESTS, E_MAX)


def draw_self_keys(key, part):
    return key_draw(jax.random.fold_in(key, 17), REQUESTS, S_MAX).astype(jnp.bfloat16)


def draw_cross_keys(key, part):
    return key_draw(jax.random.fold_in(key, 19), REQUESTS, E_MAX).astype(jnp.bfloat16)


def set_ends(array, key, smallest, top_value):
    extent = array.shape
    spot = [jax.random.randint(jax.random.fold_in(key, axis), (), 0, extent[axis]) for axis in range(len(extent))]
    array = array.at[tuple(spot)].set(smallest)
    longest = extent.index(max(extent))
    spot[longest] = (spot[longest] + 1) % extent[longest]
    return array.at[tuple(spot)].set(top_value)


def shard_levels(own_key, shape, shards, least, largest):
    level, own = 1.0, jax.random.fold_in(own_key, 6)
    for dim, parts in shards:
        heights = jnp.exp(jax.random.uniform(jax.random.fold_in(own, dim), (parts,), jnp.float32, least / len(shards), largest / len(shards)))
        level = level * jnp.repeat(heights, shape[dim] // parts).reshape([-1 if axis == dim else 1 for axis in range(len(shape))])
    return level


def scatter_about(stream_key, dims, width, reach, cuts=(), held_as=jnp.bfloat16):
    loudness = shard_levels(stream_key, dims, cuts, -0.22, 0.18) if cuts else 1.0
    entries = jax.random.normal(stream_key, dims, jnp.float32) * width * loudness
    return jnp.minimum(jnp.maximum(entries, -reach), reach).astype(held_as)


def setup_inputs(seed: int = 0) -> dict:
    key_list = jax.random.split(jax.random.key(seed), 20)
    tokens = scatter_about(key_list[0], (REQUESTS, D), 1.0, 6.0, ((0, 64),))
    self_keys = draw_self_keys(jax.random.fold_in(key_list[19], 71), 0)
    self_values = scatter_about(key_list[2], (REQUESTS, S_MAX, D), 1.0, 6.0, ((0, 64), (2, 8)))
    self_len = draw_self_len(jax.random.fold_in(key_list[19], 71), 0)
    cross_keys = draw_cross_keys(jax.random.fold_in(key_list[19], 71), 0)
    cross_values = scatter_about(key_list[5], (REQUESTS, E_MAX, D), 1.0, 6.0, ((0, 64), (2, 8)))
    cross_len = draw_cross_len(jax.random.fold_in(key_list[19], 71), 0)
    give_slot = set_ends(jax.random.randint(key_list[7], (MOVES,), 0, REQ_DEV), jax.random.fold_in(key_list[7], 1), 0, REQ_DEV - 1).astype(jnp.int32)
    w_query = scatter_about(key_list[8], (D, D), D ** -0.5, 0.1875, ((1, 8),))
    w_key = scatter_about(key_list[9], (D, D), D ** -0.5, 0.1875, ((1, 8),))
    w_value = scatter_about(key_list[10], (D, D), D ** -0.5, 0.1875, ((1, 8),))
    w_out = scatter_about(key_list[11], (D, D), D ** -0.5, 0.1875, ((0, 8),))
    w_cross_query = scatter_about(key_list[12], (D, D), D ** -0.5, 0.1875, ((1, 8),))
    w_cross_out = scatter_about(key_list[13], (D, D), D ** -0.5, 0.1875, ((0, 8),))
    w_up = scatter_about(key_list[14], (D, FF), D ** -0.5, 0.1875, ((1, 8),))
    w_down = scatter_about(key_list[15], (FF, D), FF ** -0.5, 0.09375, ((0, 8),))
    gain_self = jnp.clip(1.0 + 0.18 * jax.random.normal(key_list[16], (D,), jnp.float32), 0.1, 1.9)
    gain_cross = jnp.clip(1.0 + 0.18 * jax.random.normal(key_list[17], (D,), jnp.float32), 0.1, 1.9)
    gain_final = jnp.clip(1.0 + 0.18 * jax.random.normal(key_list[18], (D,), jnp.float32), 0.1, 1.9)
    return {"tokens": tokens, "self_keys": self_keys, "self_values": self_values, "self_len": self_len, "cross_keys": cross_keys, "cross_values": cross_values, "cross_len": cross_len, "give_slot": give_slot, "w_query": w_query, "w_key": w_key, "w_value": w_value, "w_out": w_out, "w_cross_query": w_cross_query, "w_cross_out": w_cross_out, "w_up": w_up, "w_down": w_down, "gain_self": gain_self, "gain_cross": gain_cross, "gain_final": gain_final}


def rounded(value):
    return lax.optimization_barrier(value.astype(jnp.bfloat16)).astype(jnp.float32)

def layer_norm(value, gain):
    mean = lax.optimization_barrier(jnp.mean(value, axis=-1, keepdims=True))
    centred = value - mean
    spread = lax.optimization_barrier(jnp.mean(centred * centred, axis=-1, keepdims=True))
    return centred * lax.rsqrt(spread + 1e-05) * gain

def project(left, right):
    return jnp.dot(left, right, preferred_element_type=jnp.float32)

def attend_fresh(inputs):
    query, keys, values, length, fresh_key, fresh_value = inputs
    qf = query.astype(jnp.float32)
    scores = jnp.einsum('hd,shd->hs', qf, keys.astype(jnp.float32))
    places = jnp.arange(keys.shape[0], dtype=jnp.int32)
    scores = jnp.where(places[None, :] < length, scores, -jnp.inf)
    own = lax.optimization_barrier(jnp.sum(qf * fresh_key.astype(jnp.float32), axis=1))
    top = jnp.maximum(lax.optimization_barrier(jnp.max(scores, axis=1)), own)
    weights = jnp.exp(scores - top[:, None])
    own_weight = jnp.exp(own - top)
    total = lax.optimization_barrier(jnp.sum(weights, axis=1)) + own_weight
    mixed = jnp.einsum('hs,shd->hd', rounded(weights), values.astype(jnp.float32))
    mixed = mixed + rounded(own_weight)[:, None] * fresh_value.astype(jnp.float32)
    return (mixed / total[:, None]).astype(jnp.bfloat16)

def attend_plain(inputs):
    query, keys, values, length = inputs
    scores = jnp.einsum('hd,shd->hs', query.astype(jnp.float32), keys.astype(jnp.float32))
    places = jnp.arange(keys.shape[0], dtype=jnp.int32)
    scores = jnp.where(places[None, :] < length, scores, -jnp.inf)
    top = lax.optimization_barrier(jnp.max(scores, axis=1))
    weights = jnp.exp(scores - top[:, None])
    total = lax.optimization_barrier(jnp.sum(weights, axis=1))
    mixed = jnp.einsum('hs,shd->hd', rounded(weights), values.astype(jnp.float32))
    return (mixed / total[:, None]).astype(jnp.bfloat16)

def reference(tokens, self_keys, self_values, self_len, cross_keys, cross_values, cross_len, give_slot, w_query, w_key, w_value, w_out, w_cross_query, w_cross_out, w_up, w_down, gain_self, gain_cross, gain_final):
    scale = HEAD_DIM ** (-0.5)
    count = tokens.shape[0]
    query = (project(tokens, w_query) * scale).astype(jnp.bfloat16)
    fresh_keys = project(tokens, w_key).astype(jnp.bfloat16)
    fresh_values = project(tokens, w_value).astype(jnp.bfloat16)
    heads = (count, HEADS, HEAD_DIM)
    self_mixed = lax.map(attend_fresh, (query.reshape(heads), self_keys.reshape(count, S_MAX, HEADS, HEAD_DIM), self_values.reshape(count, S_MAX, HEADS, HEAD_DIM), self_len, fresh_keys.reshape(heads), fresh_values.reshape(heads)))
    first = layer_norm(tokens.astype(jnp.float32) + project(self_mixed.reshape(count, D), w_out), gain_self).astype(jnp.bfloat16)
    cross_query = (project(first, w_cross_query) * scale).astype(jnp.bfloat16)
    cross_mixed = lax.map(attend_plain, (cross_query.reshape(heads), cross_keys.reshape(count, E_MAX, HEADS, HEAD_DIM), cross_values.reshape(count, E_MAX, HEADS, HEAD_DIM), cross_len))
    second = layer_norm(first.astype(jnp.float32) + project(cross_mixed.reshape(count, D), w_cross_out), gain_cross).astype(jnp.bfloat16)
    hidden = jax.nn.gelu(project(second, w_up), approximate=False).astype(jnp.bfloat16)
    layer_out = layer_norm(second.astype(jnp.float32) + project(hidden, w_down), gain_final).astype(jnp.bfloat16)
    index = jnp.arange(REQUESTS, dtype=jnp.int32)
    device = index // REQ_DEV
    slot_of = index % REQ_DEV
    partner = (device + MOVES // 2) % MOVES
    source = jnp.where(slot_of == give_slot[device], partner * REQ_DEV + give_slot[partner], index).astype(jnp.int32)
    decoded = layer_out[source]
    new_keys = fresh_keys[source]
    new_values = fresh_values[source]
    devices = jnp.arange(MOVES, dtype=jnp.int32)
    giver = (devices + MOVES // 2) % MOVES
    arrivals = (giver * REQ_DEV + give_slot[giver]).astype(jnp.int32)
    moved_keys = self_keys[arrivals]
    moved_values = self_values[arrivals]
    return (decoded, new_keys, new_values, moved_keys, moved_values)
```

```python
import jax
import jax.numpy as jnp
from jax import lax
from jax.sharding import PartitionSpec as P

HEAD_DIM = 64


def passed_along(block, axis, distance):
    devices = range(lax.axis_size(axis))
    route = [((i - distance) % len(devices), i) for i in devices]
    return lax.ppermute(block, axis, route)


def layer_norm(value, gain):
    mean = jnp.mean(value, axis=-1, keepdims=True)
    centred = value - mean
    spread = jnp.mean(centred * centred, axis=-1, keepdims=True)
    return centred * lax.rsqrt(spread + 1e-05) * gain


def attend(query, keys, values, lengths, fresh_key, fresh_value):
    count, span, width = keys.shape
    heads = width // HEAD_DIM
    block = min(512, span)
    query_heads = query.reshape(count, heads, HEAD_DIM)
    steps = (jnp.max(lengths) + block - 1) // block
    places = lax.iota(jnp.int32, block)

    def score_block(index, board):
        start = index * block
        piece = keys.reshape(count, block, heads, HEAD_DIM)
        scores = jnp.einsum("qhd,qshd->qhs", query_heads, piece, preferred_element_type=jnp.float32)
        valid = (start + places)[None, None, :] < lengths[:, None, None]
        scores = jnp.where(valid, scores, -jnp.inf)
        return scores

    board = lax.fori_loop(
        0, steps, score_block, jnp.full((count, heads, span), -jnp.inf, jnp.float32)
    )
    top = jnp.max(board, axis=2)
    if fresh_key is not None:
        own = jnp.sum(
            query_heads.astype(jnp.float32)
            * fresh_key.reshape(count, heads, HEAD_DIM).astype(jnp.float32),
            axis=2,
        )
        top = jnp.maximum(top, own)
    weights_all = jnp.exp(board - top[:, :, None])
    total = jnp.sum(weights_all, axis=2)

    def mix_block(index, accum):
        weights = weights_all.astype(jnp.bfloat16)
        piece = values.reshape(count, block, heads, HEAD_DIM)
        return accum + jnp.einsum(
            "qhs,qshd->qhd", weights, piece, preferred_element_type=jnp.float32
        )

    mixed = lax.fori_loop(0, steps, mix_block, jnp.zeros((count, heads, HEAD_DIM), jnp.float32))
    if fresh_key is not None:
        own_weight = jnp.exp(own - top)
        total = total + own_weight
        mixed = mixed + own_weight.astype(jnp.bfloat16).astype(jnp.float32)[
            :, :, None
        ] * fresh_value.reshape(count, heads, HEAD_DIM).astype(jnp.float32)
    return (mixed / total[:, :, None]).astype(jnp.bfloat16).reshape(count, width)


def decode_layer(
    tokens, self_keys, self_values, self_len, cross_keys, cross_values, cross_len, params
):
    (
        w_query,
        w_key,
        w_value,
        w_out,
        w_cross_query,
        w_cross_out,
        w_up,
        w_down,
        gain_self,
        gain_cross,
        gain_final,
    ) = params
    scale = HEAD_DIM ** (-0.5)
    query = (jnp.dot(tokens, w_query, preferred_element_type=jnp.float32) * scale).astype(
        jnp.bfloat16
    )
    fresh_keys = jnp.dot(tokens, w_key, preferred_element_type=jnp.float32).astype(jnp.bfloat16)
    fresh_values = jnp.dot(tokens, w_value, preferred_element_type=jnp.float32).astype(jnp.bfloat16)
    self_mixed = attend(query, self_keys, self_values, self_len, fresh_keys, fresh_values)
    self_total = lax.psum(jnp.dot(self_mixed, w_out, preferred_element_type=jnp.float32), "head")
    first = layer_norm(tokens.astype(jnp.float32) + self_total, gain_self).astype(jnp.bfloat16)
    cross_query = (
        jnp.dot(first, w_cross_query, preferred_element_type=jnp.float32) * scale
    ).astype(jnp.bfloat16)
    cross_mixed = attend(cross_query, cross_keys, cross_values, cross_len, None, None)
    cross_total = lax.psum(
        jnp.dot(cross_mixed, w_cross_out, preferred_element_type=jnp.float32), "head"
    )
    second = layer_norm(first.astype(jnp.float32) + cross_total, gain_cross).astype(jnp.bfloat16)
    hidden = jax.nn.gelu(
        jnp.dot(second, w_up, preferred_element_type=jnp.float32), approximate=False
    ).astype(jnp.bfloat16)
    ffn_total = lax.psum(jnp.dot(hidden, w_down, preferred_element_type=jnp.float32), "head")
    layer_out = layer_norm(second.astype(jnp.float32) + ffn_total, gain_final).astype(jnp.bfloat16)
    return (layer_out, fresh_keys, fresh_values)


def take_slot(array, chosen):
    return lax.dynamic_slice_in_dim(array, chosen, 1, 0)


def put_slot(array, row, chosen):
    return lax.dynamic_update_slice_in_dim(array, row, chosen, 0)


def on_device(
    tokens,
    self_keys,
    self_values,
    self_len,
    cross_keys,
    cross_values,
    cross_len,
    give_slot,
    w_query,
    w_key,
    w_value,
    w_out,
    w_cross_query,
    w_cross_out,
    w_up,
    w_down,
    gain_self,
    gain_cross,
    gain_final,
):
    params = (
        w_query,
        w_key,
        w_value,
        w_out,
        w_cross_query,
        w_cross_out,
        w_up,
        w_down,
        gain_self,
        gain_cross,
        gain_final,
    )
    chosen = give_slot[0]
    half_axis = lax.axis_size("req") // 2
    moved_keys, moved_values = passed_along(
        (take_slot(self_keys, chosen), take_slot(self_values, chosen)), "req", half_axis
    )
    layer_out, fresh_keys, fresh_values = decode_layer(
        tokens, self_keys, self_values, self_len, cross_keys, cross_values, cross_len, params
    )
    arrived = passed_along(
        (
            take_slot(layer_out, chosen),
            take_slot(fresh_keys, chosen),
            take_slot(fresh_values, chosen),
        ),
        "req",
        half_axis,
    )
    decoded = put_slot(layer_out, arrived[0], chosen)
    new_keys = put_slot(fresh_keys, arrived[1], chosen)
    new_values = put_slot(fresh_values, arrived[2], chosen)
    return (decoded, new_keys, new_values, moved_keys, moved_values)


def solution(mesh):
    placed = (
        P("req", None),
        P("req", None, "head"),
        P("req", None, "head"),
        P("req"),
        P("req", None, "head"),
        P("req", None, "head"),
        P("req"),
        P("req"),
        P(None, "head"),
        P(None, "head"),
        P(None, "head"),
        P("head", None),
        P(None, "head"),
        P("head", None),
        P(None, "head"),
        P("head", None),
        P(),
        P(),
        P(),
    )
    return jax.shard_map(
        on_device,
        mesh=mesh,
        in_specs=placed,
        out_specs=(
            P("req", None),
            P("req", "head"),
            P("req", "head"),
            P("req", None, "head"),
            P("req", None, "head"),
        ),
        check_vma=False,
    )
```

```python
import jax
import jax.numpy as jnp
from jax import lax
from jax.sharding import PartitionSpec as P

HEAD_DIM = 64


def passed_along(block, axis, distance):
    devices = range(lax.axis_size(axis))
    route = [((i - distance) % len(devices), i) for i in devices]
    return lax.ppermute(block, axis, route)


def head_sum(value):
    count = lax.axis_size("head")
    if count & (count - 1):
        return lax.psum(value, "head")
    stride = 1
    while stride < count:
        route = [(i, i ^ stride) for i in range(count)]
        value = value + lax.ppermute(value, "head", route)
        stride *= 2
    return value


def layer_norm(value, gain):
    mean = jnp.mean(value, axis=-1, keepdims=True)
    centred = value - mean
    spread = jnp.mean(centred * centred, axis=-1, keepdims=True)
    return centred * lax.rsqrt(spread + 1e-05) * gain


def attend(query, keys, values, lengths, fresh_key, fresh_value):
    count, span, width = keys.shape
    heads = width // HEAD_DIM
    block = min(512, span)
    query_heads = query.reshape(count, heads, HEAD_DIM)
    steps = (jnp.max(lengths) + block - 1) // block
    places = lax.iota(jnp.int32, block)

    def score_block(index, board):
        start = index * block
        piece = keys.reshape(count, block, heads, HEAD_DIM)
        scores = jnp.einsum("qhd,qshd->qhs", query_heads, piece, preferred_element_type=jnp.float32)
        valid = (start + places)[None, None, :] < lengths[:, None, None]
        scores = jnp.where(valid, scores, -jnp.inf)
        return scores

    board = lax.fori_loop(
        0, steps, score_block, jnp.full((count, heads, span), -jnp.inf, jnp.float32)
    )
    top = jnp.max(board, axis=2)
    if fresh_key is not None:
        own = jnp.sum(
            query_heads.astype(jnp.float32)
            * fresh_key.reshape(count, heads, HEAD_DIM).astype(jnp.float32),
            axis=2,
        )
        top = jnp.maximum(top, own)
    weights_all = jnp.exp(board - top[:, :, None])
    total = jnp.sum(weights_all, axis=2)

    def mix_block(index, accum):
        weights = weights_all.astype(jnp.bfloat16)
        piece = values.reshape(count, block, heads, HEAD_DIM)
        return accum + jnp.einsum(
            "qhs,qshd->qhd", weights, piece, preferred_element_type=jnp.float32
        )

    mixed = lax.fori_loop(0, steps, mix_block, jnp.zeros((count, heads, HEAD_DIM), jnp.float32))
    if fresh_key is not None:
        own_weight = jnp.exp(own - top)
        total = total + own_weight
        mixed = mixed + own_weight.astype(jnp.bfloat16).astype(jnp.float32)[
            :, :, None
        ] * fresh_value.reshape(count, heads, HEAD_DIM).astype(jnp.float32)
    return (mixed / total[:, :, None]).astype(jnp.bfloat16).reshape(count, width)


def decode_layer(
    tokens, self_keys, self_values, self_len, cross_keys, cross_values, cross_len, params
):
    (
        w_query,
        w_key,
        w_value,
        w_out,
        w_cross_query,
        w_cross_out,
        w_up,
        w_down,
        gain_self,
        gain_cross,
        gain_final,
    ) = params
    scale = HEAD_DIM ** (-0.5)
    query = (jnp.dot(tokens, w_query, preferred_element_type=jnp.float32) * scale).astype(
        jnp.bfloat16
    )
    fresh_keys = jnp.dot(tokens, w_key, preferred_element_type=jnp.float32).astype(jnp.bfloat16)
    fresh_values = jnp.dot(tokens, w_value, preferred_element_type=jnp.float32).astype(jnp.bfloat16)
    self_mixed = attend(query, self_keys, self_values, self_len, fresh_keys, fresh_values)
    self_total = head_sum(jnp.dot(self_mixed, w_out, preferred_element_type=jnp.float32))
    first = layer_norm(tokens.astype(jnp.float32) + self_total, gain_self).astype(jnp.bfloat16)
    cross_query = (
        jnp.dot(first, w_cross_query, preferred_element_type=jnp.float32) * scale
    ).astype(jnp.bfloat16)
    cross_mixed = attend(cross_query, cross_keys, cross_values, cross_len, None, None)
    cross_total = head_sum(
        jnp.dot(cross_mixed, w_cross_out, preferred_element_type=jnp.float32)
    )
    second = layer_norm(first.astype(jnp.float32) + cross_total, gain_cross).astype(jnp.bfloat16)
    hidden = jax.nn.gelu(
        jnp.dot(second, w_up, preferred_element_type=jnp.float32), approximate=False
    ).astype(jnp.bfloat16)
    ffn_total = head_sum(jnp.dot(hidden, w_down, preferred_element_type=jnp.float32))
    layer_out = layer_norm(second.astype(jnp.float32) + ffn_total, gain_final).astype(jnp.bfloat16)
    return (layer_out, fresh_keys, fresh_values)


def take_slot(array, chosen):
    return lax.dynamic_slice_in_dim(array, chosen, 1, 0)


def put_slot(array, row, chosen):
    return lax.dynamic_update_slice_in_dim(array, row, chosen, 0)


def on_device(
    tokens,
    self_keys,
    self_values,
    self_len,
    cross_keys,
    cross_values,
    cross_len,
    give_slot,
    w_query,
    w_key,
    w_value,
    w_out,
    w_cross_query,
    w_cross_out,
    w_up,
    w_down,
    gain_self,
    gain_cross,
    gain_final,
):
    params = (
        w_query,
        w_key,
        w_value,
        w_out,
        w_cross_query,
        w_cross_out,
        w_up,
        w_down,
        gain_self,
        gain_cross,
        gain_final,
    )
    chosen = give_slot[0]
    half_axis = lax.axis_size("req") // 2
    caches = jnp.concatenate((take_slot(self_keys, chosen), take_slot(self_values, chosen)), axis=0)
    moved = passed_along(caches, "req", half_axis)
    moved_keys, moved_values = moved[:1], moved[1:]
    layer_out, fresh_keys, fresh_values = decode_layer(
        tokens, self_keys, self_values, self_len, cross_keys, cross_values, cross_len, params
    )
    width = layer_out.shape[1]
    part = fresh_keys.shape[1]
    rows = jnp.concatenate(
        (
            take_slot(layer_out, chosen),
            take_slot(fresh_keys, chosen),
            take_slot(fresh_values, chosen),
        ),
        axis=1,
    )
    arrived = passed_along(rows, "req", half_axis)
    decoded = put_slot(layer_out, arrived[:, :width], chosen)
    new_keys = put_slot(fresh_keys, arrived[:, width : width + part], chosen)
    new_values = put_slot(fresh_values, arrived[:, width + part :], chosen)
    return (decoded, new_keys, new_values, moved_keys, moved_values)


def solution(mesh):
    placed = (
        P("req", None),
        P("req", None, "head"),
        P("req", None, "head"),
        P("req"),
        P("req", None, "head"),
        P("req", None, "head"),
        P("req"),
        P("req"),
        P(None, "head"),
        P(None, "head"),
        P(None, "head"),
        P("head", None),
        P(None, "head"),
        P("head", None),
        P(None, "head"),
        P("head", None),
        P(),
        P(),
        P(),
    )
    return jax.shard_map(
        on_device,
        mesh=mesh,
        in_specs=placed,
        out_specs=(
            P("req", None),
            P("req", "head"),
            P("req", "head"),
            P("req", None, "head"),
            P("req", None, "head"),
        ),
        check_vma=False,
    )
```

```python
import jax
import jax.numpy as jnp
from jax import lax
from jax.sharding import PartitionSpec as P

HEAD_DIM = 64


def passed_along(block, axis, distance):
    devices = range(lax.axis_size(axis))
    route = [((i - distance) % len(devices), i) for i in devices]
    return lax.ppermute(block, axis, route)


def head_sum(value):
    count = lax.axis_size("head")
    spread = jnp.broadcast_to(value[None], (count,) + value.shape)
    gathered = lax.all_to_all(spread, "head", 0, 0)
    return jnp.sum(gathered, axis=0)


def layer_norm(value, gain):
    mean = jnp.mean(value, axis=-1, keepdims=True)
    centred = value - mean
    spread = jnp.mean(centred * centred, axis=-1, keepdims=True)
    return centred * lax.rsqrt(spread + 1e-05) * gain


def attend(query, keys, values, lengths, fresh_key, fresh_value):
    count, span, width = keys.shape
    heads = width // HEAD_DIM
    block = min(512, span)
    query_heads = query.reshape(count, heads, HEAD_DIM)
    steps = (jnp.max(lengths) + block - 1) // block
    places = lax.iota(jnp.int32, block)

    def score_block(index, board):
        start = index * block
        piece = keys.reshape(count, block, heads, HEAD_DIM)
        scores = jnp.einsum("qhd,qshd->qhs", query_heads, piece, preferred_element_type=jnp.float32)
        valid = (start + places)[None, None, :] < lengths[:, None, None]
        scores = jnp.where(valid, scores, -jnp.inf)
        return scores

    board = lax.fori_loop(
        0, steps, score_block, jnp.full((count, heads, span), -jnp.inf, jnp.float32)
    )
    top = jnp.max(board, axis=2)
    if fresh_key is not None:
        own = jnp.sum(
            query_heads.astype(jnp.float32)
            * fresh_key.reshape(count, heads, HEAD_DIM).astype(jnp.float32),
            axis=2,
        )
        top = jnp.maximum(top, own)
    weights_all = jnp.exp(board - top[:, :, None])
    total = jnp.sum(weights_all, axis=2)

    def mix_block(index, accum):
        weights = weights_all.astype(jnp.bfloat16)
        piece = values.reshape(count, block, heads, HEAD_DIM)
        return accum + jnp.einsum(
            "qhs,qshd->qhd", weights, piece, preferred_element_type=jnp.float32
        )

    mixed = lax.fori_loop(0, steps, mix_block, jnp.zeros((count, heads, HEAD_DIM), jnp.float32))
    if fresh_key is not None:
        own_weight = jnp.exp(own - top)
        total = total + own_weight
        mixed = mixed + own_weight.astype(jnp.bfloat16).astype(jnp.float32)[
            :, :, None
        ] * fresh_value.reshape(count, heads, HEAD_DIM).astype(jnp.float32)
    return (mixed / total[:, :, None]).astype(jnp.bfloat16).reshape(count, width)


def decode_layer(
    tokens, self_keys, self_values, self_len, cross_keys, cross_values, cross_len, params
):
    (
        w_query,
        w_key,
        w_value,
        w_out,
        w_cross_query,
        w_cross_out,
        w_up,
        w_down,
        gain_self,
        gain_cross,
        gain_final,
    ) = params
    scale = HEAD_DIM ** (-0.5)
    query = (jnp.dot(tokens, w_query, preferred_element_type=jnp.float32) * scale).astype(
        jnp.bfloat16
    )
    fresh_keys = jnp.dot(tokens, w_key, preferred_element_type=jnp.float32).astype(jnp.bfloat16)
    fresh_values = jnp.dot(tokens, w_value, preferred_element_type=jnp.float32).astype(jnp.bfloat16)
    self_mixed = attend(query, self_keys, self_values, self_len, fresh_keys, fresh_values)
    self_total = head_sum(jnp.dot(self_mixed, w_out, preferred_element_type=jnp.float32))
    first = layer_norm(tokens.astype(jnp.float32) + self_total, gain_self).astype(jnp.bfloat16)
    cross_query = (
        jnp.dot(first, w_cross_query, preferred_element_type=jnp.float32) * scale
    ).astype(jnp.bfloat16)
    cross_mixed = attend(cross_query, cross_keys, cross_values, cross_len, None, None)
    cross_total = head_sum(
        jnp.dot(cross_mixed, w_cross_out, preferred_element_type=jnp.float32)
    )
    second = layer_norm(first.astype(jnp.float32) + cross_total, gain_cross).astype(jnp.bfloat16)
    hidden = jax.nn.gelu(
        jnp.dot(second, w_up, preferred_element_type=jnp.float32), approximate=False
    ).astype(jnp.bfloat16)
    ffn_total = head_sum(jnp.dot(hidden, w_down, preferred_element_type=jnp.float32))
    layer_out = layer_norm(second.astype(jnp.float32) + ffn_total, gain_final).astype(jnp.bfloat16)
    return (layer_out, fresh_keys, fresh_values)


def take_slot(array, chosen):
    return lax.dynamic_slice_in_dim(array, chosen, 1, 0)


def put_slot(array, row, chosen):
    return lax.dynamic_update_slice_in_dim(array, row, chosen, 0)


def on_device(
    tokens,
    self_keys,
    self_values,
    self_len,
    cross_keys,
    cross_values,
    cross_len,
    give_slot,
    w_query,
    w_key,
    w_value,
    w_out,
    w_cross_query,
    w_cross_out,
    w_up,
    w_down,
    gain_self,
    gain_cross,
    gain_final,
):
    params = (
        w_query,
        w_key,
        w_value,
        w_out,
        w_cross_query,
        w_cross_out,
        w_up,
        w_down,
        gain_self,
        gain_cross,
        gain_final,
    )
    chosen = give_slot[0]
    half_axis = lax.axis_size("req") // 2
    caches = jnp.concatenate((take_slot(self_keys, chosen), take_slot(self_values, chosen)), axis=0)
    moved = passed_along(caches, "req", half_axis)
    moved_keys, moved_values = moved[:1], moved[1:]
    layer_out, fresh_keys, fresh_values = decode_layer(
        tokens, self_keys, self_values, self_len, cross_keys, cross_values, cross_len, params
    )
    width = layer_out.shape[1]
    part = fresh_keys.shape[1]
    rows = jnp.concatenate(
        (
            take_slot(layer_out, chosen),
            take_slot(fresh_keys, chosen),
            take_slot(fresh_values, chosen),
        ),
        axis=1,
    )
    arrived = passed_along(rows, "req", half_axis)
    decoded = put_slot(layer_out, arrived[:, :width], chosen)
    new_keys = put_slot(fresh_keys, arrived[:, width : width + part], chosen)
    new_values = put_slot(fresh_values, arrived[:, width + part :], chosen)
    return (decoded, new_keys, new_values, moved_keys, moved_values)


def solution(mesh):
    placed = (
        P("req", None),
        P("req", None, "head"),
        P("req", None, "head"),
        P("req"),
        P("req", None, "head"),
        P("req", None, "head"),
        P("req"),
        P("req"),
        P(None, "head"),
        P(None, "head"),
        P(None, "head"),
        P("head", None),
        P(None, "head"),
        P("head", None),
        P(None, "head"),
        P("head", None),
        P(),
        P(),
        P(),
    )
    return jax.shard_map(
        on_device,
        mesh=mesh,
        in_specs=placed,
        out_specs=(
            P("req", None),
            P("req", "head"),
            P("req", "head"),
            P("req", None, "head"),
            P("req", None, "head"),
        ),
        check_vma=False,
    )
```

```python
import jax
import jax.numpy as jnp
from jax import lax
from jax.sharding import PartitionSpec as P

HEAD_DIM = 64


def passed_along(block, axis, distance):
    devices = range(lax.axis_size(axis))
    route = [((i - distance) % len(devices), i) for i in devices]
    return lax.ppermute(block, axis, route)


def head_sum(value):
    count = lax.axis_size("head")
    spread = jnp.broadcast_to(value[None], (count,) + value.shape)
    gathered = lax.all_to_all(spread, "head", 0, 0)
    return jnp.sum(gathered, axis=0)


def layer_norm(value, gain):
    mean = jnp.mean(value, axis=-1, keepdims=True)
    centred = value - mean
    spread = jnp.mean(centred * centred, axis=-1, keepdims=True)
    return centred * lax.rsqrt(spread + 1e-05) * gain


def attend(query, keys, values, lengths, fresh_key, fresh_value):
    count, span, width = keys.shape
    heads = width // HEAD_DIM
    query_heads = query.reshape(count, heads, HEAD_DIM)
    key_heads = keys.reshape(count, span, heads, HEAD_DIM)
    value_heads = values.reshape(count, span, heads, HEAD_DIM)
    scores = jnp.einsum(
        "qhd,qshd->qhs", query_heads, key_heads, preferred_element_type=jnp.float32
    )
    valid = lax.iota(jnp.int32, span)[None, None, :] < lengths[:, None, None]
    scores = jnp.where(valid, scores, -jnp.inf)
    top = jnp.max(scores, axis=2)
    if fresh_key is not None:
        own = jnp.sum(
            query_heads.astype(jnp.float32)
            * fresh_key.reshape(count, heads, HEAD_DIM).astype(jnp.float32),
            axis=2,
        )
        top = jnp.maximum(top, own)
    weights = jnp.exp(scores - top[:, :, None])
    total = jnp.sum(weights, axis=2)
    mixed = jnp.einsum(
        "qhs,qshd->qhd",
        weights.astype(jnp.bfloat16),
        value_heads,
        preferred_element_type=jnp.float32,
    )
    if fresh_key is not None:
        own_weight = jnp.exp(own - top)
        total = total + own_weight
        mixed = mixed + own_weight.astype(jnp.bfloat16).astype(jnp.float32)[
            :, :, None
        ] * fresh_value.reshape(count, heads, HEAD_DIM).astype(jnp.float32)
    return (mixed / total[:, :, None]).astype(jnp.bfloat16).reshape(count, width)


def decode_layer(
    tokens, self_keys, self_values, self_len, cross_keys, cross_values, cross_len, params
):
    (
        w_query,
        w_key,
        w_value,
        w_out,
        w_cross_query,
        w_cross_out,
        w_up,
        w_down,
        gain_self,
        gain_cross,
        gain_final,
    ) = params
    scale = HEAD_DIM ** (-0.5)
    query = (jnp.dot(tokens, w_query, preferred_element_type=jnp.float32) * scale).astype(
        jnp.bfloat16
    )
    fresh_keys = jnp.dot(tokens, w_key, preferred_element_type=jnp.float32).astype(jnp.bfloat16)
    fresh_values = jnp.dot(tokens, w_value, preferred_element_type=jnp.float32).astype(jnp.bfloat16)
    self_mixed = attend(query, self_keys, self_values, self_len, fresh_keys, fresh_values)
    self_total = head_sum(jnp.dot(self_mixed, w_out, preferred_element_type=jnp.float32))
    first = layer_norm(tokens.astype(jnp.float32) + self_total, gain_self).astype(jnp.bfloat16)
    cross_query = (
        jnp.dot(first, w_cross_query, preferred_element_type=jnp.float32) * scale
    ).astype(jnp.bfloat16)
    cross_mixed = attend(cross_query, cross_keys, cross_values, cross_len, None, None)
    cross_total = head_sum(
        jnp.dot(cross_mixed, w_cross_out, preferred_element_type=jnp.float32)
    )
    second = layer_norm(first.astype(jnp.float32) + cross_total, gain_cross).astype(jnp.bfloat16)
    hidden = jax.nn.gelu(
        jnp.dot(second, w_up, preferred_element_type=jnp.float32), approximate=False
    ).astype(jnp.bfloat16)
    ffn_total = head_sum(jnp.dot(hidden, w_down, preferred_element_type=jnp.float32))
    layer_out = layer_norm(second.astype(jnp.float32) + ffn_total, gain_final).astype(jnp.bfloat16)
    return (layer_out, fresh_keys, fresh_values)


def take_slot(array, chosen):
    return lax.dynamic_slice_in_dim(array, chosen, 1, 0)


def put_slot(array, row, chosen):
    return lax.dynamic_update_slice_in_dim(array, row, chosen, 0)


def on_device(
    tokens,
    self_keys,
    self_values,
    self_len,
    cross_keys,
    cross_values,
    cross_len,
    give_slot,
    w_query,
    w_key,
    w_value,
    w_out,
    w_cross_query,
    w_cross_out,
    w_up,
    w_down,
    gain_self,
    gain_cross,
    gain_final,
):
    params = (
        w_query,
        w_key,
        w_value,
        w_out,
        w_cross_query,
        w_cross_out,
        w_up,
        w_down,
        gain_self,
        gain_cross,
        gain_final,
    )
    chosen = give_slot[0]
    half_axis = lax.axis_size("req") // 2
    layer_out, fresh_keys, fresh_values = decode_layer(
        tokens, self_keys, self_values, self_len, cross_keys, cross_values, cross_len, params
    )
    count, span, part = self_keys.shape
    width = layer_out.shape[1]
    rows = jnp.concatenate(
        (
            take_slot(layer_out, chosen),
            take_slot(fresh_keys, chosen),
            take_slot(fresh_values, chosen),
        ),
        axis=1,
    ).reshape(-1, part)
    parcel = jnp.concatenate(
        (
            take_slot(self_keys, chosen).reshape(span, part),
            take_slot(self_values, chosen).reshape(span, part),
            rows,
        ),
        axis=0,
    )
    arrived = passed_along(parcel, "req", half_axis)
    moved_keys = arrived[:span].reshape(1, span, part)
    moved_values = arrived[span : 2 * span].reshape(1, span, part)
    arrived_rows = arrived[2 * span :].reshape(1, -1)
    decoded = put_slot(layer_out, arrived_rows[:, :width], chosen)
    new_keys = put_slot(fresh_keys, arrived_rows[:, width : width + part], chosen)
    new_values = put_slot(fresh_values, arrived_rows[:, width + part :], chosen)
    return (decoded, new_keys, new_values, moved_keys, moved_values)


def solution(mesh):
    placed = (
        P("req", None),
        P("req", None, "head"),
        P("req", None, "head"),
        P("req"),
        P("req", None, "head"),
        P("req", None, "head"),
        P("req"),
        P("req"),
        P(None, "head"),
        P(None, "head"),
        P(None, "head"),
        P("head", None),
        P(None, "head"),
        P("head", None),
        P(None, "head"),
        P("head", None),
        P(),
        P(),
        P(),
    )
    step = jax.shard_map(
        on_device,
        mesh=mesh,
        in_specs=placed,
        out_specs=(
            P("req", None),
            P("req", "head"),
            P("req", "head"),
            P("req", None, "head"),
            P("req", None, "head"),
        ),
        check_vma=False,
    )
    return step
```

```python
import jax
import jax.numpy as jnp
from jax import lax
from jax.sharding import PartitionSpec as P

HEAD_DIM = 64


def head_sum(value):
    count = lax.axis_size("head")
    spread = jnp.broadcast_to(value[None], (count,) + value.shape)
    gathered = lax.all_to_all(spread, "head", 0, 0)
    return jnp.sum(gathered, axis=0)


def layer_norm(value, gain):
    mean = jnp.mean(value, axis=-1, keepdims=True)
    centred = value - mean
    spread = jnp.mean(centred * centred, axis=-1, keepdims=True)
    return centred * lax.rsqrt(spread + 1e-05) * gain


def attend(query, keys, values, lengths, fresh_key, fresh_value):
    count, span, width = keys.shape
    heads = width // HEAD_DIM
    query_heads = query.reshape(count, heads, HEAD_DIM)
    key_heads = keys.reshape(count, span, heads, HEAD_DIM)
    value_heads = values.reshape(count, span, heads, HEAD_DIM)
    scores = jnp.einsum(
        "qhd,qshd->qhs", query_heads, key_heads, preferred_element_type=jnp.float32
    )
    valid = lax.iota(jnp.int32, span)[None, None, :] < lengths[:, None, None]
    scores = jnp.where(valid, scores, -jnp.inf)
    top = jnp.max(scores, axis=2)
    if fresh_key is not None:
        own = jnp.sum(
            query_heads.astype(jnp.float32)
            * fresh_key.reshape(count, heads, HEAD_DIM).astype(jnp.float32),
            axis=2,
        )
        top = jnp.maximum(top, own)
    weights = jnp.exp(scores - top[:, :, None])
    total = jnp.sum(weights, axis=2)
    mixed = jnp.einsum(
        "qhs,qshd->qhd",
        weights.astype(jnp.bfloat16),
        value_heads,
        preferred_element_type=jnp.float32,
    )
    if fresh_key is not None:
        own_weight = jnp.exp(own - top)
        total = total + own_weight
        mixed = mixed + own_weight.astype(jnp.bfloat16).astype(jnp.float32)[
            :, :, None
        ] * fresh_value.reshape(count, heads, HEAD_DIM).astype(jnp.float32)
    return (mixed / total[:, :, None]).astype(jnp.bfloat16).reshape(count, width)


def decode_layer(
    tokens, self_keys, self_values, self_len, cross_keys, cross_values, cross_len, params
):
    (
        w_query,
        w_key,
        w_value,
        w_out,
        w_cross_query,
        w_cross_out,
        w_up,
        w_down,
        gain_self,
        gain_cross,
        _,
    ) = params
    scale = HEAD_DIM ** (-0.5)
    query = (jnp.dot(tokens, w_query, preferred_element_type=jnp.float32) * scale).astype(
        jnp.bfloat16
    )
    fresh_keys = jnp.dot(tokens, w_key, preferred_element_type=jnp.float32).astype(jnp.bfloat16)
    fresh_values = jnp.dot(tokens, w_value, preferred_element_type=jnp.float32).astype(jnp.bfloat16)
    self_mixed = attend(query, self_keys, self_values, self_len, fresh_keys, fresh_values)
    self_total = head_sum(jnp.dot(self_mixed, w_out, preferred_element_type=jnp.float32))
    first = layer_norm(tokens.astype(jnp.float32) + self_total, gain_self).astype(jnp.bfloat16)
    cross_query = (
        jnp.dot(first, w_cross_query, preferred_element_type=jnp.float32) * scale
    ).astype(jnp.bfloat16)
    cross_mixed = attend(cross_query, cross_keys, cross_values, cross_len, None, None)
    cross_total = head_sum(
        jnp.dot(cross_mixed, w_cross_out, preferred_element_type=jnp.float32)
    )
    second = layer_norm(first.astype(jnp.float32) + cross_total, gain_cross).astype(jnp.bfloat16)
    hidden = jax.nn.gelu(
        jnp.dot(second, w_up, preferred_element_type=jnp.float32), approximate=False
    ).astype(jnp.bfloat16)
    ffn_part = jnp.dot(hidden, w_down, preferred_element_type=jnp.float32)
    return (second, ffn_part, fresh_keys, fresh_values)


def take_slot(array, chosen):
    return lax.dynamic_slice_in_dim(array, chosen, 1, 0)


def put_slot(array, row, chosen):
    return lax.dynamic_update_slice_in_dim(array, row, chosen, 0)


def on_device(
    tokens,
    self_keys,
    self_values,
    self_len,
    cross_keys,
    cross_values,
    cross_len,
    give_slot,
    w_query,
    w_key,
    w_value,
    w_out,
    w_cross_query,
    w_cross_out,
    w_up,
    w_down,
    gain_self,
    gain_cross,
    gain_final,
):
    params = (
        w_query,
        w_key,
        w_value,
        w_out,
        w_cross_query,
        w_cross_out,
        w_up,
        w_down,
        gain_self,
        gain_cross,
        gain_final,
    )
    chosen = give_slot[0]
    kept = 1 - chosen
    flip = [(0, 1), (1, 0)]
    heads = lax.axis_size("head")
    second, ffn_part, fresh_keys, fresh_values = decode_layer(
        tokens, self_keys, self_values, self_len, cross_keys, cross_values, cross_len, params
    )
    _, span, part = self_keys.shape
    parcel = jnp.concatenate(
        (
            take_slot(self_keys, chosen).reshape(span, part),
            take_slot(self_values, chosen).reshape(span, part),
            take_slot(fresh_keys, chosen),
            take_slot(fresh_values, chosen),
        ),
        axis=0,
    )
    arrived = lax.ppermute(parcel, "zh", flip)
    partner_second = lax.ppermute(take_slot(second, chosen), "zh", flip)
    moved_keys = arrived[:span].reshape(1, span, part)
    moved_values = arrived[span : 2 * span].reshape(1, span, part)
    new_keys = put_slot(fresh_keys, arrived[2 * span : 2 * span + 1], chosen)
    new_values = put_slot(fresh_values, arrived[2 * span + 1 :], chosen)
    side = lax.axis_index("zh")
    mine = (lax.iota(jnp.int32, 2) == side)[:, None, None, None]
    chunks = jnp.where(
        mine, take_slot(ffn_part, kept)[None, None], take_slot(ffn_part, chosen)[None, None]
    )
    chunks = jnp.broadcast_to(chunks, (2, heads) + chunks.shape[2:])
    chunks = chunks.reshape((2 * heads,) + chunks.shape[2:])
    gathered = lax.all_to_all(chunks, ("zh", "head"), 0, 0)
    gathered = gathered.reshape((2, heads) + gathered.shape[1:])
    own_sum = jnp.sum(lax.dynamic_index_in_dim(gathered, side, 0, keepdims=False), axis=0)
    far_sum = jnp.sum(lax.dynamic_index_in_dim(gathered, 1 - side, 0, keepdims=False), axis=0)
    own_out = layer_norm(take_slot(second, kept).astype(jnp.float32) + own_sum, gain_final)
    far_out = layer_norm(partner_second.astype(jnp.float32) + far_sum, gain_final)
    decoded = put_slot(
        put_slot(second, own_out.astype(jnp.bfloat16), kept),
        far_out.astype(jnp.bfloat16),
        chosen,
    )
    return (decoded, new_keys, new_values, moved_keys, moved_values)


def solution(mesh):
    req = mesh.shape["req"]
    split = jax.sharding.Mesh(
        mesh.devices.reshape(2, req // 2, mesh.shape["head"]), ("zh", "zl", "head")
    )
    placed = (
        P(("zh", "zl"), None),
        P(("zh", "zl"), None, "head"),
        P(("zh", "zl"), None, "head"),
        P(("zh", "zl")),
        P(("zh", "zl"), None, "head"),
        P(("zh", "zl"), None, "head"),
        P(("zh", "zl")),
        P(("zh", "zl")),
        P(None, "head"),
        P(None, "head"),
        P(None, "head"),
        P("head", None),
        P(None, "head"),
        P("head", None),
        P(None, "head"),
        P("head", None),
        P(),
        P(),
        P(),
    )
    return jax.shard_map(
        on_device,
        mesh=split,
        in_specs=placed,
        out_specs=(
            P(("zh", "zl"), None),
            P(("zh", "zl"), "head"),
            P(("zh", "zl"), "head"),
            P(("zh", "zl"), None, "head"),
            P(("zh", "zl"), None, "head"),
        ),
        check_vma=False,
    )
```

```python
import jax
import jax.numpy as jnp
from jax import lax
from jax.sharding import PartitionSpec as P

HEAD_DIM = 64


def passed_along(block, axis, distance):
    devices = range(lax.axis_size(axis))
    route = [((i - distance) % len(devices), i) for i in devices]
    return lax.ppermute(block, axis, route)


def head_sum(value):
    count = lax.axis_size("head")
    spread = jnp.broadcast_to(value[None], (count,) + value.shape)
    gathered = lax.all_to_all(spread, "head", 0, 0)
    return jnp.sum(gathered, axis=0)


def layer_norm(value, gain):
    mean = jnp.mean(value, axis=-1, keepdims=True)
    centred = value - mean
    spread = jnp.mean(centred * centred, axis=-1, keepdims=True)
    return centred * lax.rsqrt(spread + 1e-05) * gain


def attend(query, keys, values, lengths, fresh_key, fresh_value):
    count, span, width = keys.shape
    heads = width // HEAD_DIM
    owner = lax.iota(jnp.int32, width) // HEAD_DIM
    pick = owner[:, None] == lax.iota(jnp.int32, heads)[None, :]
    query_blocks = jnp.where(pick[None], query[:, :, None], jnp.zeros((), query.dtype))
    scores = jnp.einsum(
        "qsd,qdh->qsh", keys, query_blocks, preferred_element_type=jnp.float32
    )
    valid = lax.iota(jnp.int32, span)[None, :, None] < lengths[:, None, None]
    scores = jnp.where(valid, scores, -jnp.inf)
    top = jnp.max(scores, axis=1)
    if fresh_key is not None:
        own = jnp.sum(
            query.reshape(count, heads, HEAD_DIM).astype(jnp.float32)
            * fresh_key.reshape(count, heads, HEAD_DIM).astype(jnp.float32),
            axis=2,
        )
        top = jnp.maximum(top, own)
    weights = jnp.exp(scores - top[:, None, :])
    total = jnp.sum(weights, axis=1)
    mixed_all = jnp.einsum(
        "qsh,qsd->qhd",
        weights.astype(jnp.bfloat16),
        values,
        preferred_element_type=jnp.float32,
    )
    mixed = jnp.sum(jnp.where(pick.T[None], mixed_all, 0.0), axis=1)
    if fresh_key is not None:
        own_weight = jnp.exp(own - top)
        total = total + own_weight
        mixed = mixed + jnp.repeat(
            own_weight.astype(jnp.bfloat16).astype(jnp.float32), HEAD_DIM, axis=1
        ) * fresh_value.astype(jnp.float32)
    return (mixed / jnp.repeat(total, HEAD_DIM, axis=1)).astype(jnp.bfloat16)


def decode_layer(
    tokens, self_keys, self_values, self_len, cross_keys, cross_values, cross_len, params
):
    (
        w_query,
        w_key,
        w_value,
        w_out,
        w_cross_query,
        w_cross_out,
        w_up,
        w_down,
        gain_self,
        gain_cross,
        gain_final,
    ) = params
    scale = HEAD_DIM ** (-0.5)
    query = (jnp.dot(tokens, w_query, preferred_element_type=jnp.float32) * scale).astype(
        jnp.bfloat16
    )
    fresh_keys = jnp.dot(tokens, w_key, preferred_element_type=jnp.float32).astype(jnp.bfloat16)
    fresh_values = jnp.dot(tokens, w_value, preferred_element_type=jnp.float32).astype(jnp.bfloat16)
    self_mixed = attend(query, self_keys, self_values, self_len, fresh_keys, fresh_values)
    self_total = head_sum(jnp.dot(self_mixed, w_out, preferred_element_type=jnp.float32))
    first = layer_norm(tokens.astype(jnp.float32) + self_total, gain_self).astype(jnp.bfloat16)
    cross_query = (
        jnp.dot(first, w_cross_query, preferred_element_type=jnp.float32) * scale
    ).astype(jnp.bfloat16)
    cross_mixed = attend(cross_query, cross_keys, cross_values, cross_len, None, None)
    cross_total = head_sum(
        jnp.dot(cross_mixed, w_cross_out, preferred_element_type=jnp.float32)
    )
    second = layer_norm(first.astype(jnp.float32) + cross_total, gain_cross).astype(jnp.bfloat16)
    hidden = jax.nn.gelu(
        jnp.dot(second, w_up, preferred_element_type=jnp.float32), approximate=False
    ).astype(jnp.bfloat16)
    ffn_total = head_sum(jnp.dot(hidden, w_down, preferred_element_type=jnp.float32))
    layer_out = layer_norm(second.astype(jnp.float32) + ffn_total, gain_final).astype(jnp.bfloat16)
    return (layer_out, fresh_keys, fresh_values)


def take_slot(array, chosen):
    return lax.dynamic_slice_in_dim(array, chosen, 1, 0)


def put_slot(array, row, chosen):
    return lax.dynamic_update_slice_in_dim(array, row, chosen, 0)


def on_device(
    tokens,
    self_keys,
    self_values,
    self_len,
    cross_keys,
    cross_values,
    cross_len,
    give_slot,
    w_query,
    w_key,
    w_value,
    w_out,
    w_cross_query,
    w_cross_out,
    w_up,
    w_down,
    gain_self,
    gain_cross,
    gain_final,
):
    params = (
        w_query,
        w_key,
        w_value,
        w_out,
        w_cross_query,
        w_cross_out,
        w_up,
        w_down,
        gain_self,
        gain_cross,
        gain_final,
    )
    chosen = give_slot[0]
    half_axis = lax.axis_size("req") // 2
    caches = jnp.concatenate((take_slot(self_keys, chosen), take_slot(self_values, chosen)), axis=0)
    moved = passed_along(caches, "req", half_axis)
    moved_keys, moved_values = moved[:1], moved[1:]
    layer_out, fresh_keys, fresh_values = decode_layer(
        tokens, self_keys, self_values, self_len, cross_keys, cross_values, cross_len, params
    )
    width = layer_out.shape[1]
    part = fresh_keys.shape[1]
    rows = jnp.concatenate(
        (
            take_slot(layer_out, chosen),
            take_slot(fresh_keys, chosen),
            take_slot(fresh_values, chosen),
        ),
        axis=1,
    )
    arrived = passed_along(rows, "req", half_axis)
    decoded = put_slot(layer_out, arrived[:, :width], chosen)
    new_keys = put_slot(fresh_keys, arrived[:, width : width + part], chosen)
    new_values = put_slot(fresh_values, arrived[:, width + part :], chosen)
    return (decoded, new_keys, new_values, moved_keys, moved_values)


def solution(mesh):
    placed = (
        P("req", None),
        P("req", None, "head"),
        P("req", None, "head"),
        P("req"),
        P("req", None, "head"),
        P("req", None, "head"),
        P("req"),
        P("req"),
        P(None, "head"),
        P(None, "head"),
        P(None, "head"),
        P("head", None),
        P(None, "head"),
        P("head", None),
        P(None, "head"),
        P("head", None),
        P(),
        P(),
        P(),
    )
    return jax.shard_map(
        on_device,
        mesh=mesh,
        in_specs=placed,
        out_specs=(
            P("req", None),
            P("req", "head"),
            P("req", "head"),
            P("req", None, "head"),
            P("req", None, "head"),
        ),
        check_vma=False,
    )
```

```python
import jax
import jax.numpy as jnp
from jax import lax
from jax.sharding import PartitionSpec as P

HEAD_DIM = 64


def passed_along(block, axis, distance):
    devices = range(lax.axis_size(axis))
    route = [((i - distance) % len(devices), i) for i in devices]
    return lax.ppermute(block, axis, route)


def head_sum(value):
    count = lax.axis_size("head")
    spread = jnp.broadcast_to(value[None], (count,) + value.shape)
    gathered = lax.all_to_all(spread, "head", 0, 0)
    return jnp.sum(gathered, axis=0)


def layer_norm(value, gain):
    mean = jnp.mean(value, axis=-1, keepdims=True)
    centred = value - mean
    spread = jnp.mean(centred * centred, axis=-1, keepdims=True)
    return centred * lax.rsqrt(spread + 1e-05) * gain


def attend(query, keys, values, lengths, fresh_key, fresh_value):
    count, span, width = keys.shape
    heads = width // HEAD_DIM
    query_heads = query.reshape(count, heads, HEAD_DIM)
    key_heads = keys.reshape(count, span, heads, HEAD_DIM)
    value_heads = values.reshape(count, span, heads, HEAD_DIM)
    scores = jnp.einsum(
        "qhd,qshd->qhs", query_heads, key_heads, preferred_element_type=jnp.float32
    )
    valid = lax.iota(jnp.int32, span)[None, None, :] < lengths[:, None, None]
    scores = jnp.where(valid, scores, -jnp.inf)
    top = jnp.max(scores, axis=2)
    if fresh_key is not None:
        own = jnp.sum(
            query_heads.astype(jnp.float32)
            * fresh_key.reshape(count, heads, HEAD_DIM).astype(jnp.float32),
            axis=2,
        )
        top = jnp.maximum(top, own)
    weights = jnp.exp(scores - top[:, :, None])
    total = jnp.sum(weights, axis=2)
    mixed = jnp.einsum(
        "qhs,qshd->qhd",
        weights.astype(jnp.bfloat16),
        value_heads,
        preferred_element_type=jnp.float32,
    )
    if fresh_key is not None:
        own_weight = jnp.exp(own - top)
        total = total + own_weight
        mixed = mixed + own_weight.astype(jnp.bfloat16).astype(jnp.float32)[
            :, :, None
        ] * fresh_value.reshape(count, heads, HEAD_DIM).astype(jnp.float32)
    return (mixed / total[:, :, None]).astype(jnp.bfloat16).reshape(count, width)


def decode_layer(
    tokens, self_keys, self_values, self_len, cross_keys, cross_values, cross_len, params
):
    (
        w_query,
        w_key,
        w_value,
        w_out,
        w_cross_query,
        w_cross_out,
        w_up,
        w_down,
        gain_self,
        gain_cross,
        gain_final,
    ) = params
    scale = HEAD_DIM ** (-0.5)
    query = (jnp.dot(tokens, w_query, preferred_element_type=jnp.float32) * scale).astype(
        jnp.bfloat16
    )
    fresh_keys = jnp.dot(tokens, w_key, preferred_element_type=jnp.float32).astype(jnp.bfloat16)
    fresh_values = jnp.dot(tokens, w_value, preferred_element_type=jnp.float32).astype(jnp.bfloat16)
    self_mixed = attend(query, self_keys, self_values, self_len, fresh_keys, fresh_values)
    self_total = head_sum(jnp.dot(self_mixed, w_out, preferred_element_type=jnp.float32))
    first = layer_norm(tokens.astype(jnp.float32) + self_total, gain_self).astype(jnp.bfloat16)
    cross_query = (
        jnp.dot(first, w_cross_query, preferred_element_type=jnp.float32) * scale
    ).astype(jnp.bfloat16)
    cross_mixed = attend(cross_query, cross_keys, cross_values, cross_len, None, None)
    cross_total = head_sum(
        jnp.dot(cross_mixed, w_cross_out, preferred_element_type=jnp.float32)
    )
    second = layer_norm(first.astype(jnp.float32) + cross_total, gain_cross).astype(jnp.bfloat16)
    hidden = jax.nn.gelu(
        jnp.dot(second, w_up, preferred_element_type=jnp.float32), approximate=False
    ).astype(jnp.bfloat16)
    ffn_total = head_sum(jnp.dot(hidden, w_down, preferred_element_type=jnp.float32))
    layer_out = layer_norm(second.astype(jnp.float32) + ffn_total, gain_final).astype(jnp.bfloat16)
    return (layer_out, fresh_keys, fresh_values)


def take_slot(array, chosen):
    return lax.dynamic_slice_in_dim(array, chosen, 1, 0)


def on_device(
    tokens,
    self_keys,
    self_values,
    self_len,
    cross_keys,
    cross_values,
    cross_len,
    give_slot,
    w_query,
    w_key,
    w_value,
    w_out,
    w_cross_query,
    w_cross_out,
    w_up,
    w_down,
    gain_self,
    gain_cross,
    gain_final,
):
    params = (
        w_query,
        w_key,
        w_value,
        w_out,
        w_cross_query,
        w_cross_out,
        w_up,
        w_down,
        gain_self,
        gain_cross,
        gain_final,
    )
    chosen = give_slot[0]
    half_axis = lax.axis_size("req") // 2
    count, span, part = self_keys.shape
    layer_out, fresh_keys, fresh_values = decode_layer(
        tokens, self_keys, self_values, self_len, cross_keys, cross_values, cross_len, params
    )
    parcel = jnp.concatenate(
        (
            take_slot(self_keys, chosen).reshape(span, part),
            take_slot(self_values, chosen).reshape(span, part),
            take_slot(fresh_keys, chosen),
            take_slot(fresh_values, chosen),
        ),
        axis=0,
    )
    arrived = passed_along(parcel, "req", half_axis)
    moved_keys = arrived[:span].reshape(1, span, part)
    moved_values = arrived[span : 2 * span].reshape(1, span, part)
    here = (lax.iota(jnp.int32, count) == chosen)[:, None]
    new_keys = jnp.where(here, arrived[2 * span : 2 * span + 1], fresh_keys)
    new_values = jnp.where(here, arrived[2 * span + 1 :], fresh_values)
    row = passed_along(take_slot(layer_out, chosen), "req", half_axis)
    decoded = jnp.where(here, row, layer_out)
    return (decoded, new_keys, new_values, moved_keys, moved_values)


def solution(mesh):
    placed = (
        P("req", None),
        P("req", None, "head"),
        P("req", None, "head"),
        P("req"),
        P("req", None, "head"),
        P("req", None, "head"),
        P("req"),
        P("req"),
        P(None, "head"),
        P(None, "head"),
        P(None, "head"),
        P("head", None),
        P(None, "head"),
        P("head", None),
        P(None, "head"),
        P("head", None),
        P(),
        P(),
        P(),
    )
    return jax.shard_map(
        on_device,
        mesh=mesh,
        in_specs=placed,
        out_specs=(
            P("req", None),
            P("req", "head"),
            P("req", "head"),
            P("req", None, "head"),
            P("req", None, "head"),
        ),
        check_vma=False,
    )
```

```python
import jax
import jax.numpy as jnp
from jax import lax
from jax.sharding import PartitionSpec as P

HEAD_DIM = 64


def passed_along(block, axis, distance):
    devices = range(lax.axis_size(axis))
    route = [((i - distance) % len(devices), i) for i in devices]
    return lax.ppermute(block, axis, route)


def head_sum(value):
    value = value + lax.ppermute(value, "hc", [(0, 1), (1, 0)])
    count = lax.axis_size("hy")
    spread = jnp.broadcast_to(value[None], (count,) + value.shape)
    gathered = lax.all_to_all(spread, "hy", 0, 0)
    return jnp.sum(gathered, axis=0)


def layer_norm(value, gain):
    mean = jnp.mean(value, axis=-1, keepdims=True)
    centred = value - mean
    spread = jnp.mean(centred * centred, axis=-1, keepdims=True)
    return centred * lax.rsqrt(spread + 1e-05) * gain


def attend(query, keys, values, lengths, fresh_key, fresh_value):
    count, span, width = keys.shape
    heads = width // HEAD_DIM
    query_heads = query.reshape(count, heads, HEAD_DIM)
    key_heads = keys.reshape(count, span, heads, HEAD_DIM)
    value_heads = values.reshape(count, span, heads, HEAD_DIM)
    scores = jnp.einsum(
        "qhd,qshd->qhs", query_heads, key_heads, preferred_element_type=jnp.float32
    )
    valid = lax.iota(jnp.int32, span)[None, None, :] < lengths[:, None, None]
    scores = jnp.where(valid, scores, -jnp.inf)
    top = jnp.max(scores, axis=2)
    if fresh_key is not None:
        own = jnp.sum(
            query_heads.astype(jnp.float32)
            * fresh_key.reshape(count, heads, HEAD_DIM).astype(jnp.float32),
            axis=2,
        )
        top = jnp.maximum(top, own)
    weights = jnp.exp(scores - top[:, :, None])
    total = jnp.sum(weights, axis=2)
    mixed = jnp.einsum(
        "qhs,qshd->qhd",
        weights.astype(jnp.bfloat16),
        value_heads,
        preferred_element_type=jnp.float32,
    )
    if fresh_key is not None:
        own_weight = jnp.exp(own - top)
        total = total + own_weight
        mixed = mixed + own_weight.astype(jnp.bfloat16).astype(jnp.float32)[
            :, :, None
        ] * fresh_value.reshape(count, heads, HEAD_DIM).astype(jnp.float32)
    return (mixed / total[:, :, None]).astype(jnp.bfloat16).reshape(count, width)


def decode_layer(
    tokens, self_keys, self_values, self_len, cross_keys, cross_values, cross_len, params
):
    (
        w_query,
        w_key,
        w_value,
        w_out,
        w_cross_query,
        w_cross_out,
        w_up,
        w_down,
        gain_self,
        gain_cross,
        gain_final,
    ) = params
    scale = HEAD_DIM ** (-0.5)
    query = (jnp.dot(tokens, w_query, preferred_element_type=jnp.float32) * scale).astype(
        jnp.bfloat16
    )
    fresh_keys = jnp.dot(tokens, w_key, preferred_element_type=jnp.float32).astype(jnp.bfloat16)
    fresh_values = jnp.dot(tokens, w_value, preferred_element_type=jnp.float32).astype(jnp.bfloat16)
    self_mixed = attend(query, self_keys, self_values, self_len, fresh_keys, fresh_values)
    self_total = head_sum(jnp.dot(self_mixed, w_out, preferred_element_type=jnp.float32))
    first = layer_norm(tokens.astype(jnp.float32) + self_total, gain_self).astype(jnp.bfloat16)
    cross_query = (
        jnp.dot(first, w_cross_query, preferred_element_type=jnp.float32) * scale
    ).astype(jnp.bfloat16)
    cross_mixed = attend(cross_query, cross_keys, cross_values, cross_len, None, None)
    cross_total = head_sum(
        jnp.dot(cross_mixed, w_cross_out, preferred_element_type=jnp.float32)
    )
    second = layer_norm(first.astype(jnp.float32) + cross_total, gain_cross).astype(jnp.bfloat16)
    hidden = jax.nn.gelu(
        jnp.dot(second, w_up, preferred_element_type=jnp.float32), approximate=False
    ).astype(jnp.bfloat16)
    ffn_total = head_sum(jnp.dot(hidden, w_down, preferred_element_type=jnp.float32))
    layer_out = layer_norm(second.astype(jnp.float32) + ffn_total, gain_final).astype(jnp.bfloat16)
    return (layer_out, fresh_keys, fresh_values)


def take_slot(array, chosen):
    return lax.dynamic_slice_in_dim(array, chosen, 1, 0)


def put_slot(array, row, chosen):
    return lax.dynamic_update_slice_in_dim(array, row, chosen, 0)


def on_device(
    tokens,
    self_keys,
    self_values,
    self_len,
    cross_keys,
    cross_values,
    cross_len,
    give_slot,
    w_query,
    w_key,
    w_value,
    w_out,
    w_cross_query,
    w_cross_out,
    w_up,
    w_down,
    gain_self,
    gain_cross,
    gain_final,
):
    params = (
        w_query,
        w_key,
        w_value,
        w_out,
        w_cross_query,
        w_cross_out,
        w_up,
        w_down,
        gain_self,
        gain_cross,
        gain_final,
    )
    chosen = give_slot[0]
    half_axis = lax.axis_size("req") // 2
    caches = jnp.concatenate((take_slot(self_keys, chosen), take_slot(self_values, chosen)), axis=0)
    moved = passed_along(caches, "req", half_axis)
    moved_keys, moved_values = moved[:1], moved[1:]
    layer_out, fresh_keys, fresh_values = decode_layer(
        tokens, self_keys, self_values, self_len, cross_keys, cross_values, cross_len, params
    )
    width = layer_out.shape[1]
    part = fresh_keys.shape[1]
    rows = jnp.concatenate(
        (
            take_slot(layer_out, chosen),
            take_slot(fresh_keys, chosen),
            take_slot(fresh_values, chosen),
        ),
        axis=1,
    )
    arrived = passed_along(rows, "req", half_axis)
    decoded = put_slot(layer_out, arrived[:, :width], chosen)
    new_keys = put_slot(fresh_keys, arrived[:, width : width + part], chosen)
    new_values = put_slot(fresh_values, arrived[:, width + part :], chosen)
    return (decoded, new_keys, new_values, moved_keys, moved_values)


def solution(mesh):
    split = jax.sharding.Mesh(
        mesh.devices.reshape(mesh.shape["req"], mesh.shape["head"] // 2, 2), ("req", "hy", "hc")
    )
    placed = (
        P("req", None),
        P("req", None, ("hy", "hc")),
        P("req", None, ("hy", "hc")),
        P("req"),
        P("req", None, ("hy", "hc")),
        P("req", None, ("hy", "hc")),
        P("req"),
        P("req"),
        P(None, ("hy", "hc")),
        P(None, ("hy", "hc")),
        P(None, ("hy", "hc")),
        P(("hy", "hc"), None),
        P(None, ("hy", "hc")),
        P(("hy", "hc"), None),
        P(None, ("hy", "hc")),
        P(("hy", "hc"), None),
        P(),
        P(),
        P(),
    )
    return jax.shard_map(
        on_device,
        mesh=split,
        in_specs=placed,
        out_specs=(
            P("req", None),
            P("req", ("hy", "hc")),
            P("req", ("hy", "hc")),
            P("req", None, ("hy", "hc")),
            P("req", None, ("hy", "hc")),
        ),
        check_vma=False,
    )
```

```python
import jax
import jax.numpy as jnp
from jax import lax
from jax.sharding import PartitionSpec as P

HEAD_DIM = 64


def passed_along(block, axis, distance):
    devices = range(lax.axis_size(axis))
    route = [((i - distance) % len(devices), i) for i in devices]
    return lax.ppermute(block, axis, route)


def head_sum(value, tie=None):
    count = lax.axis_size("head")
    spread = jnp.broadcast_to(value[None], (count,) + value.shape)
    if tie is not None:
        tie, spread = lax.optimization_barrier((tie, spread))
    gathered = lax.all_to_all(spread, "head", 0, 0)
    return jnp.sum(gathered, axis=0), tie


def layer_norm(value, gain):
    mean = jnp.mean(value, axis=-1, keepdims=True)
    centred = value - mean
    spread = jnp.mean(centred * centred, axis=-1, keepdims=True)
    return centred * lax.rsqrt(spread + 1e-05) * gain


def attend(query, keys, values, lengths, fresh_key, fresh_value):
    count, span, width = keys.shape
    heads = width // HEAD_DIM
    query_heads = query.reshape(count, heads, HEAD_DIM)
    key_heads = keys.reshape(count, span, heads, HEAD_DIM)
    value_heads = values.reshape(count, span, heads, HEAD_DIM)
    scores = jnp.einsum(
        "qhd,qshd->qhs", query_heads, key_heads, preferred_element_type=jnp.float32
    )
    valid = lax.iota(jnp.int32, span)[None, None, :] < lengths[:, None, None]
    scores = jnp.where(valid, scores, -jnp.inf)
    top = jnp.max(scores, axis=2)
    if fresh_key is not None:
        own = jnp.sum(
            query_heads.astype(jnp.float32)
            * fresh_key.reshape(count, heads, HEAD_DIM).astype(jnp.float32),
            axis=2,
        )
        top = jnp.maximum(top, own)
    weights = jnp.exp(scores - top[:, :, None])
    total = jnp.sum(weights, axis=2)
    mixed = jnp.einsum(
        "qhs,qshd->qhd",
        weights.astype(jnp.bfloat16),
        value_heads,
        preferred_element_type=jnp.float32,
    )
    if fresh_key is not None:
        own_weight = jnp.exp(own - top)
        total = total + own_weight
        mixed = mixed + own_weight.astype(jnp.bfloat16).astype(jnp.float32)[
            :, :, None
        ] * fresh_value.reshape(count, heads, HEAD_DIM).astype(jnp.float32)
    return (mixed / total[:, :, None]).astype(jnp.bfloat16).reshape(count, width)


def decode_layer(
    tokens, self_keys, self_values, self_len, cross_keys, cross_values, cross_len, params, tie=None
):
    (
        w_query,
        w_key,
        w_value,
        w_out,
        w_cross_query,
        w_cross_out,
        w_up,
        w_down,
        gain_self,
        gain_cross,
        gain_final,
    ) = params
    scale = HEAD_DIM ** (-0.5)
    query = (jnp.dot(tokens, w_query, preferred_element_type=jnp.float32) * scale).astype(
        jnp.bfloat16
    )
    fresh_keys = jnp.dot(tokens, w_key, preferred_element_type=jnp.float32).astype(jnp.bfloat16)
    fresh_values = jnp.dot(tokens, w_value, preferred_element_type=jnp.float32).astype(jnp.bfloat16)
    self_mixed = attend(query, self_keys, self_values, self_len, fresh_keys, fresh_values)
    self_total, tie = head_sum(jnp.dot(self_mixed, w_out, preferred_element_type=jnp.float32), tie)
    first = layer_norm(tokens.astype(jnp.float32) + self_total, gain_self).astype(jnp.bfloat16)
    cross_query = (
        jnp.dot(first, w_cross_query, preferred_element_type=jnp.float32) * scale
    ).astype(jnp.bfloat16)
    cross_mixed = attend(cross_query, cross_keys, cross_values, cross_len, None, None)
    cross_total, _ = head_sum(
        jnp.dot(cross_mixed, w_cross_out, preferred_element_type=jnp.float32)
    )
    second = layer_norm(first.astype(jnp.float32) + cross_total, gain_cross).astype(jnp.bfloat16)
    hidden = jax.nn.gelu(
        jnp.dot(second, w_up, preferred_element_type=jnp.float32), approximate=False
    ).astype(jnp.bfloat16)
    ffn_total, _ = head_sum(jnp.dot(hidden, w_down, preferred_element_type=jnp.float32))
    layer_out = layer_norm(second.astype(jnp.float32) + ffn_total, gain_final).astype(jnp.bfloat16)
    return (layer_out, fresh_keys, fresh_values, tie)


def take_slot(array, chosen):
    return lax.dynamic_slice_in_dim(array, chosen, 1, 0)


def on_device(
    tokens,
    self_keys,
    self_values,
    self_len,
    cross_keys,
    cross_values,
    cross_len,
    give_slot,
    w_query,
    w_key,
    w_value,
    w_out,
    w_cross_query,
    w_cross_out,
    w_up,
    w_down,
    gain_self,
    gain_cross,
    gain_final,
):
    params = (
        w_query,
        w_key,
        w_value,
        w_out,
        w_cross_query,
        w_cross_out,
        w_up,
        w_down,
        gain_self,
        gain_cross,
        gain_final,
    )
    chosen = give_slot[0]
    half_axis = lax.axis_size("req") // 2
    caches = jnp.concatenate((take_slot(self_keys, chosen), take_slot(self_values, chosen)), axis=0)
    layer_out, fresh_keys, fresh_values, caches = decode_layer(
        tokens, self_keys, self_values, self_len, cross_keys, cross_values, cross_len, params,
        caches,
    )
    count, span, part = self_keys.shape
    parcel = jnp.concatenate(
        (
            caches.reshape(2 * span, part),
            take_slot(fresh_keys, chosen),
            take_slot(fresh_values, chosen),
        ),
        axis=0,
    )
    arrived = passed_along(parcel, "req", half_axis)
    moved_keys = arrived[:span].reshape(1, span, part)
    moved_values = arrived[span : 2 * span].reshape(1, span, part)
    here = (lax.iota(jnp.int32, count) == chosen)[:, None]
    new_keys = jnp.where(here, arrived[2 * span : 2 * span + 1], fresh_keys)
    new_values = jnp.where(here, arrived[2 * span + 1 :], fresh_values)
    row = passed_along(take_slot(layer_out, chosen), "req", half_axis)
    decoded = jnp.where(here, row, layer_out)
    return (decoded, new_keys, new_values, moved_keys, moved_values)


def solution(mesh):
    placed = (
        P("req", None),
        P("req", None, "head"),
        P("req", None, "head"),
        P("req"),
        P("req", None, "head"),
        P("req", None, "head"),
        P("req"),
        P("req"),
        P(None, "head"),
        P(None, "head"),
        P(None, "head"),
        P("head", None),
        P(None, "head"),
        P("head", None),
        P(None, "head"),
        P("head", None),
        P(),
        P(),
        P(),
    )
    return jax.shard_map(
        on_device,
        mesh=mesh,
        in_specs=placed,
        out_specs=(
            P("req", None),
            P("req", "head"),
            P("req", "head"),
            P("req", None, "head"),
            P("req", None, "head"),
        ),
        check_vma=False,
    )
```
